1024 devices in a mesh: expert: 8 (over x), dp: 128 (over y, z, core).
Axes of the slice: x: 8, y: 8, z: 8, core: 2. Of those that a mesh axis runs over, the one named last changes fastest.
Arguments:
- hidden: bfloat16 [131072, 768], P(('expert', 'dp')), may hold values from -24 to 24
- cotangent: bfloat16 [131072, 1024], P(('expert', 'dp')), may hold values from -6 to 6
- expert_ids: int32 [131072, 1], P(('expert', 'dp')), may hold values from 0 to 7; in each aligned block of 128 rows (0 to 127, 128 to 255, ...) at most 32 rows name the same one
- counts: int32 [8, 128], P('expert', 'dp'), may hold values from 64 to 128, as said below
- down_weight: bfloat16 [8, 768, 1024], P('expert', 'dp'), may hold values from -0.21875 to 0.21875
Outputs:
- output: bfloat16 [131072, 1024], P(('expert', 'dp'))
- hidden_grad: bfloat16 [131072, 768], P(('expert', 'dp'))
- weight_grad: float32 [8, 768, 1024], P('expert', 'dp')
The draws below stay inside these ranges and needn't reach their ends.
Inputs may be any that keep to these rules, and one draw needn't show every extreme that they name: `expert_ids`: in the rows of one device no expert is named more than 32 times, and some device names some expert exactly 32 times. `counts`: some device is full in every draw.
All inputs are finite; a program needn't handle non-finite values.
Results may differ from the reference program's by a relative error of at most 0.001.
Values may be sent and summed in bfloat16 or wider, within the bound.
No kernel may reach another device: no remote copies, remote signals or barrier semaphores. Data moves between devices by JAX's collectives and lax.ppermute only.
A program may use at most 32 MiB of HBM per device.

```python
import math
import jax
import jax.numpy as jnp
import numpy as np
from jax import lax

D = 1024
FF = 768
TOK_DEV = 128
CAP = 32
EXPERTS = 8
EXP_ROWS = 8
DP_ROWS = 128
TOKENS = 131072


def draw_counts(key, part):
    first, second = jax.random.split(jax.random.fold_in(key, 17))
    values = jax.random.randint(first, (EXP_ROWS * DP_ROWS,), TOK_DEV // 2, TOK_DEV + 1)
    full_at = jax.random.randint(second, (), 0, EXP_ROWS * DP_ROWS)
    values = jnp.where(jnp.arange(EXP_ROWS * DP_ROWS) == full_at, TOK_DEV, values)
    return values.reshape(EXP_ROWS, DP_ROWS).astype(jnp.int32)


def strengthened(array, stream_key, source, target, parts, factor):
    def block_of(axis_at):
        return (jnp.arange(array.shape[axis_at]) // (array.shape[axis_at] // parts)).reshape((-1,) + (1,) * (array.ndim - 1 - axis_at))

    one_side = jax.random.permutation(stream_key, parts)[block_of(target)]
    other_side = (block_of(target) + parts // 2) % parts
    return jnp.where((block_of(source) == one_side) | (block_of(source) == other_side), factor * array, array)


def shard_levels(rng, dims, cuts, least, high):
    gain, own = 1.0, jax.random.fold_in(rng, 6)
    for axis_at, blocks in cuts:
        heights = jnp.exp(jax.random.uniform(jax.random.fold_in(own, axis_at), (blocks,), jnp.float32, least / len(cuts), high / len(cuts)))
        gain = gain * jnp.repeat(heights, dims[axis_at] // blocks).reshape([-1 if axis == axis_at else 1 for axis in range(len(dims))])
    return gain


def deal_out(own_key, own, number, rows, count, top, reach, slope):
    sequence = jax.random.permutation(own_key, count)
    heavy_load, usual = shares(count, rows * top, reach, slope, True), shares(count, rows * top, reach, slope, False)
    places = jnp.arange(count)

    def named(lengths, offset_by):
        used = int((lengths > 0).sum())
        fixed = max(1, used // 4)
        moved = fixed + (places - fixed + offset_by * (used - fixed)) % max(1, count - fixed)
        return jnp.zeros((count,), jnp.int32).at[sequence[jnp.where(places < fixed, places, moved)]].set(jnp.asarray(lengths, jnp.int32))

    lengths = jnp.where(number % 4 == 0, named(heavy_load, number // 4), named(usual, number - number // 4 - 1))
    mixed = jax.random.permutation(jax.random.fold_in(own, 3), count)
    donor, sink = mixed[0:count // 2 * 2:2], mixed[1:count // 2 * 2:2]
    room = jnp.minimum(lengths[donor] - 1, reach - lengths[sink]) // 2
    room = jnp.where((donor == sequence[0]) | (sink == sequence[0]) | (lengths[sink] == 0), 0, jnp.maximum(room, 0))
    moved = jax.random.randint(jax.random.fold_in(own, 4), (count // 2,), 0, 1 << 20) % (room + 1)
    lengths = lengths.at[donor].add(-moved).at[sink].add(moved)
    members = jnp.searchsorted(jnp.cumsum(lengths), jnp.arange(rows * top), side="right").astype(jnp.int32)
    grid = members.reshape(top, rows).T
    grid = grid[jax.random.permutation(jax.random.fold_in(own, 1), rows)]
    offset_by = jax.random.randint(jax.random.fold_in(own, 2), (rows, 1), 0, top)
    return jnp.take_along_axis(grid, (jnp.arange(top)[None, :] + offset_by) % top, axis=1)


def shares(number_of, total, most, slope, full):
    weights = [(1 << 20) // math.isqrt(grade ** slope) + 1 for grade in range(1, number_of + 1)]
    largest = most if full else min(most, max(-(-total // number_of), total * weights[0] // sum(weights)))
    least = 1 if total - largest >= number_of - 1 else 0
    given, rest = [largest] + [least] * (number_of - 1), total - largest - least * (number_of - 1)
    while rest > 0:
        free = [i for i in range(1, number_of) if given[i] < largest] or [i for i in range(1, number_of) if given[i] < most]
        pool, remaining = sum([weights[i] for i in free]), rest
        for i in free:
            more = min(most - given[i], max(1, remaining * weights[i] // pool), rest)
            given[i] = given[i] + more
            rest = rest - more
    return np.array(given)


def scatter_about(own_key, shape, scale, most, cuts=(), kind=jnp.bfloat16):
    gain = shard_levels(own_key, shape, cuts, -0.22, 0.18) if cuts else 1.0
    entries = jax.random.normal(own_key, shape, jnp.float32) * scale * gain
    return jnp.minimum(jnp.maximum(entries, -most), most).astype(kind)


def noise_with(own_key, extent, spread, most, cuts, heavy, kind=jnp.bfloat16):
    array = spread * jax.random.normal(own_key, extent, jnp.float32)
    if cuts:
        array = array * shard_levels(own_key, extent, cuts, -0.22, 0.18)
    return jnp.clip(strengthened(array, jax.random.fold_in(own_key, 3), *heavy), -most, most).astype(kind)


def setup_inputs(seed: int = 0) -> dict:
    key_of = jax.random.split(jax.random.key(seed), 6)
    hidden = noise_with(key_of[0], (TOKENS, FF), 1.0, 24.0, ((0, 1024),), (0, 1, 256, 6.0))
    cotangent = scatter_about(key_of[1], (TOKENS, D), 1.0, 6.0, ((0, 1024),))
    expert_ids_keys = jax.random.split(jax.random.fold_in(key_of[2], 1), TOKENS // TOK_DEV)
    expert_ids_turns = jax.random.permutation(jax.random.fold_in(key_of[2], 3), TOKENS // TOK_DEV)
    expert_ids = jax.vmap(lambda own, number: deal_out(jax.random.fold_in(key_of[2], 2), own, number, TOK_DEV, EXPERTS, 1, CAP, 2))(expert_ids_keys, expert_ids_turns).reshape((TOKENS, 1))
    counts = draw_counts(jax.random.fold_in(key_of[5], 71), 0)
    down_weight = scatter_about(key_of[4], (EXPERTS, FF, D), FF ** -0.5, 0.21875, ((0, 8), (1, 128)))
    return dict(hidden=hidden, cotangent=cotangent, expert_ids=expert_ids, counts=counts, down_weight=down_weight)


def reference(hidden, cotangent, expert_ids, counts, down_weight):
    tokens_all = hidden.shape[0]
    experts = down_weight.shape[0]
    per_dev = tokens_all // counts.size
    bound = counts.size * CAP
    ids = expert_ids[:, 0].astype(jnp.int32)
    places = jnp.arange(tokens_all, dtype=jnp.int32)
    limit = jnp.repeat(counts.reshape(-1).astype(jnp.int32), per_dev)
    live = (places % per_dev) < limit

    def one_expert(carry, which):
        out_acc, grad_acc = carry
        chosen = jnp.logical_and(ids == which, live)
        rank = jnp.cumsum(chosen.astype(jnp.int32)) - 1
        index = jnp.where(chosen, rank, bound).astype(jnp.int32)
        h_buf = jnp.zeros((bound, hidden.shape[1]), jnp.bfloat16).at[index].set(hidden, mode="drop")
        g_buf = jnp.zeros((bound, cotangent.shape[1]), jnp.bfloat16).at[index].set(cotangent, mode="drop")
        weight = lax.dynamic_index_in_dim(down_weight, which, 0, keepdims=False)
        y_buf = jnp.dot(h_buf, weight, preferred_element_type=jnp.float32).astype(jnp.bfloat16)
        dh_buf = lax.dot_general(g_buf, weight, (((1,), (1,)), ((), ())), preferred_element_type=jnp.float32).astype(jnp.bfloat16)
        grad = lax.dot_general(h_buf, g_buf, (((0,), (0,)), ((), ())), preferred_element_type=jnp.float32)
        safe = jnp.minimum(index, bound - 1).astype(jnp.int32)
        out_acc = jnp.where(chosen[:, None], y_buf[safe], out_acc)
        grad_acc = jnp.where(chosen[:, None], dh_buf[safe], grad_acc)
        return (out_acc, grad_acc), grad

    start = (jnp.zeros(cotangent.shape, jnp.bfloat16), jnp.zeros(hidden.shape, jnp.bfloat16))
    (output, hidden_grad), weight_grad = lax.scan(one_expert, start, jnp.arange(experts, dtype=jnp.int32))
    return output, hidden_grad, weight_grad
```

```python
import jax
import jax.numpy as jnp
from jax import lax
from jax.sharding import Mesh
from jax.sharding import PartitionSpec as P

CAP = 32
DP = ("y", "z", "c")


def on_device(hidden, cotangent, expert_ids, counts, down_weight):
    tok_rows, ff = hidden.shape
    d = cotangent.shape[1]
    groups = lax.axis_size("expert")
    ny, nz, nc = lax.axis_size("y"), lax.axis_size("z"), lax.axis_size("c")
    width = groups * CAP
    ids = expert_ids[:, 0]
    live = jnp.arange(tok_rows, dtype=jnp.int32) < counts[0, 0]
    member = (ids[:, None] == jnp.arange(groups, dtype=jnp.int32)[None, :]).astype(jnp.int32)
    rank = jnp.sum((jnp.cumsum(member, 0) - 1) * member, 1)
    target = ids * CAP + rank
    placing = jnp.logical_and(
        target[None, :] == jnp.arange(width, dtype=jnp.int32)[:, None], live[None, :]
    ).astype(jnp.bfloat16)
    both = jnp.concatenate([hidden, cotangent], axis=1)
    send = (
        jnp.dot(placing, both, preferred_element_type=jnp.float32)
        .astype(jnp.bfloat16)
        .reshape(groups, CAP, ff + d)
    )
    weight = lax.all_gather(down_weight, DP, axis=1, tiled=True)[0]
    recv = lax.all_to_all(send, "expert", split_axis=0, concat_axis=0, tiled=True).reshape(width, ff + d)
    h_rows = recv[:, :ff]
    g_rows = recv[:, ff:]
    rows_dev = ff // (ny * nz * nc)
    h_perm = h_rows.reshape(width, ny, nz, nc, rows_dev).transpose(0, 3, 2, 1, 4).reshape(width, ff)
    partial_grad = lax.dot_general(
        h_perm, g_rows, (((0,), (0,)), ((), ())), preferred_element_type=jnp.float32
    )
    summed = partial_grad
    for axis, n in (("c", nc), ("z", nz), ("y", ny)):
        parts = lax.all_to_all(
            summed.reshape(n, summed.shape[0] // n, d), axis, split_axis=0, concat_axis=0, tiled=True
        )
        summed = jnp.sum(parts, axis=0)
    y_rows = jnp.dot(h_rows, weight, preferred_element_type=jnp.float32).astype(jnp.bfloat16)
    dh_rows = lax.dot_general(
        g_rows, weight, (((1,), (1,)), ((), ())), preferred_element_type=jnp.float32
    ).astype(jnp.bfloat16)
    back = lax.all_to_all(
        jnp.concatenate([y_rows, dh_rows], axis=1).reshape(groups, CAP, d + ff),
        "expert",
        split_axis=0,
        concat_axis=0,
        tiled=True,
    ).reshape(width, d + ff)
    output = lax.dot_general(
        placing, back[:, :d], (((0,), (0,)), ((), ())), preferred_element_type=jnp.float32
    ).astype(jnp.bfloat16)
    hidden_grad = lax.dot_general(
        placing, back[:, d:], (((0,), (0,)), ((), ())), preferred_element_type=jnp.float32
    ).astype(jnp.bfloat16)
    return (output, hidden_grad, summed[None])


def solution(mesh):
    ex, dp = mesh.devices.shape
    view = Mesh(mesh.devices.reshape(ex, dp // 16, 8, 2), ("expert",) + DP)
    tokens = P(("expert",) + DP, None)
    placed = (tokens, tokens, tokens, P("expert", DP), P("expert", DP, None))
    return jax.shard_map(
        on_device,
        mesh=view,
        in_specs=placed,
        out_specs=(tokens, tokens, P("expert", DP, None)),
        check_vma=False,
    )
```

```python
import jax
import jax.numpy as jnp
from jax import lax
from jax.sharding import Mesh
from jax.sharding import PartitionSpec as P

CAP = 32
DP = ("y", "z", "c")


def on_device(hidden, cotangent, expert_ids, counts, down_weight):
    tok_rows, ff = hidden.shape
    d = cotangent.shape[1]
    groups = lax.axis_size("expert")
    ny, nz, nc = lax.axis_size("y"), lax.axis_size("z"), lax.axis_size("c")
    width = groups * CAP
    ids = expert_ids[:, 0]
    live = jnp.arange(tok_rows, dtype=jnp.int32) < counts[0, 0]
    member = (ids[:, None] == jnp.arange(groups, dtype=jnp.int32)[None, :]).astype(jnp.int32)
    rank = jnp.sum((jnp.cumsum(member, 0) - 1) * member, 1)
    target = ids * CAP + rank
    placing = jnp.logical_and(
        target[None, :] == jnp.arange(width, dtype=jnp.int32)[:, None], live[None, :]
    ).astype(jnp.bfloat16)
    both = jnp.concatenate([hidden, cotangent], axis=1)
    send = (
        jnp.dot(placing, both, preferred_element_type=jnp.float32)
        .astype(jnp.bfloat16)
        .reshape(groups, CAP, ff + d)
    )
    weight = down_weight[0]
    for axis, n in (("c", nc), ("z", nz), ("y", ny)):
        weight = lax.all_to_all(
            jnp.broadcast_to(weight, (n,) + weight.shape), axis, split_axis=0, concat_axis=0, tiled=True
        ).reshape(n * weight.shape[0], d)
    recv = lax.all_to_all(send, "expert", split_axis=0, concat_axis=0, tiled=True).reshape(width, ff + d)
    h_rows = recv[:, :ff]
    g_rows = recv[:, ff:]
    rows_dev = ff // (ny * nz * nc)
    h_perm = h_rows.reshape(width, ny, nz, nc, rows_dev).transpose(0, 3, 2, 1, 4).reshape(width, ff)
    partial_grad = lax.dot_general(
        h_perm, g_rows, (((0,), (0,)), ((), ())), preferred_element_type=jnp.float32
    )
    summed = partial_grad
    for axis, n in (("c", nc), ("z", nz), ("y", ny)):
        parts = lax.all_to_all(
            summed.reshape(n, summed.shape[0] // n, d), axis, split_axis=0, concat_axis=0, tiled=True
        )
        summed = jnp.sum(parts, axis=0)
    y_rows = jnp.dot(h_rows, weight, preferred_element_type=jnp.float32).astype(jnp.bfloat16)
    dh_rows = lax.dot_general(
        g_rows, weight, (((1,), (1,)), ((), ())), preferred_element_type=jnp.float32
    ).astype(jnp.bfloat16)
    back = lax.all_to_all(
        jnp.concatenate([y_rows, dh_rows], axis=1).reshape(groups, CAP, d + ff),
        "expert",
        split_axis=0,
        concat_axis=0,
        tiled=True,
    ).reshape(width, d + ff)
    output = lax.dot_general(
        placing, back[:, :d], (((0,), (0,)), ((), ())), preferred_element_type=jnp.float32
    ).astype(jnp.bfloat16)
    hidden_grad = lax.dot_general(
        placing, back[:, d:], (((0,), (0,)), ((), ())), preferred_element_type=jnp.float32
    ).astype(jnp.bfloat16)
    return (output, hidden_grad, summed[None])


def solution(mesh):
    ex, dp = mesh.devices.shape
    view = Mesh(mesh.devices.reshape(ex, dp // 16, 8, 2), ("expert",) + DP)
    tokens = P(("expert",) + DP, None)
    placed = (tokens, tokens, tokens, P("expert", DP), P("expert", DP, None))
    return jax.shard_map(
        on_device,
        mesh=view,
        in_specs=placed,
        out_specs=(tokens, tokens, P("expert", DP, None)),
        check_vma=False,
    )
```

```python
import jax
import jax.numpy as jnp
from jax import lax
from jax.sharding import Mesh
from jax.sharding import PartitionSpec as P

CAP = 32
DP = ("y", "z", "c")


def on_device(hidden, cotangent, expert_ids, counts, down_weight):
    tok_rows, ff = hidden.shape
    d = cotangent.shape[1]
    groups = lax.axis_size("expert")
    ny, nz, nc = lax.axis_size("y"), lax.axis_size("z"), lax.axis_size("c")
    width = groups * CAP
    ids = expert_ids[:, 0]
    live = jnp.arange(tok_rows, dtype=jnp.int32) < counts[0, 0]
    member = (ids[:, None] == jnp.arange(groups, dtype=jnp.int32)[None, :]).astype(jnp.int32)
    rank = jnp.sum((jnp.cumsum(member, 0) - 1) * member, 1)
    target = ids * CAP + rank
    placing = jnp.logical_and(
        target[None, :] == jnp.arange(width, dtype=jnp.int32)[:, None], live[None, :]
    ).astype(jnp.bfloat16)
    both = jnp.concatenate([hidden, cotangent], axis=1)
    send = (
        jnp.dot(placing, both, preferred_element_type=jnp.float32)
        .astype(jnp.bfloat16)
        .reshape(groups, CAP, ff + d)
    )
    weight = lax.all_gather(down_weight, DP, axis=1, tiled=True)[0]
    recv = lax.all_to_all(send, "expert", split_axis=0, concat_axis=0, tiled=True).reshape(width, ff + d)
    h_rows = recv[:, :ff]
    g_rows = recv[:, ff:]
    rows_dev = ff // (ny * nz * nc)
    h_perm = h_rows.reshape(width, ny, nz, nc, rows_dev).transpose(0, 3, 2, 1, 4).reshape(width, ff)
    partial_grad = lax.dot_general(
        h_perm, g_rows, (((0,), (0,)), ((), ())), preferred_element_type=jnp.float32
    )
    summed = partial_grad
    for axis, n in (("c", nc), ("z", nz), ("y", ny)):
        parts = lax.all_to_all(
            summed.reshape(n, summed.shape[0] // n, d), axis, split_axis=0, concat_axis=0, tiled=True
        )
        summed = jnp.sum(parts, axis=0)
    summed, weight = lax.optimization_barrier((summed, weight))
    y_rows = jnp.dot(h_rows, weight, preferred_element_type=jnp.float32).astype(jnp.bfloat16)
    dh_rows = lax.dot_general(
        g_rows, weight, (((1,), (1,)), ((), ())), preferred_element_type=jnp.float32
    ).astype(jnp.bfloat16)
    back = lax.all_to_all(
        jnp.concatenate([y_rows, dh_rows], axis=1).reshape(groups, CAP, d + ff),
        "expert",
        split_axis=0,
        concat_axis=0,
        tiled=True,
    ).reshape(width, d + ff)
    output = lax.dot_general(
        placing, back[:, :d], (((0,), (0,)), ((), ())), preferred_element_type=jnp.float32
    ).astype(jnp.bfloat16)
    hidden_grad = lax.dot_general(
        placing, back[:, d:], (((0,), (0,)), ((), ())), preferred_element_type=jnp.float32
    ).astype(jnp.bfloat16)
    return (output, hidden_grad, summed[None])


def solution(mesh):
    ex, dp = mesh.devices.shape
    view = Mesh(mesh.devices.reshape(ex, dp // 16, 8, 2), ("expert",) + DP)
    tokens = P(("expert",) + DP, None)
    placed = (tokens, tokens, tokens, P("expert", DP), P("expert", DP, None))
    return jax.shard_map(
        on_device,
        mesh=view,
        in_specs=placed,
        out_specs=(tokens, tokens, P("expert", DP, None)),
        check_vma=False,
    )
```

```python
import jax
import jax.numpy as jnp
from jax import lax
from jax.sharding import Mesh
from jax.sharding import PartitionSpec as P

CAP = 32
DP = ("y", "z", "c")


def on_device(hidden, cotangent, expert_ids, counts, down_weight):
    tok_rows, ff = hidden.shape
    d = cotangent.shape[1]
    groups = lax.axis_size("expert")
    ny, nz, nc = lax.axis_size("y"), lax.axis_size("z"), lax.axis_size("c")
    width = groups * CAP
    ids = expert_ids[:, 0]
    live = jnp.arange(tok_rows, dtype=jnp.int32) < counts[0, 0]
    member = (ids[:, None] == jnp.arange(groups, dtype=jnp.int32)[None, :]).astype(jnp.int32)
    rank = jnp.sum((jnp.cumsum(member, 0) - 1) * member, 1)
    target = ids * CAP + rank
    placing = jnp.logical_and(
        target[None, :] == jnp.arange(width, dtype=jnp.int32)[:, None], live[None, :]
    ).astype(jnp.bfloat16)
    both = jnp.concatenate([hidden, cotangent], axis=1)
    send = (
        jnp.dot(placing, both, preferred_element_type=jnp.float32)
        .astype(jnp.bfloat16)
        .reshape(groups, CAP, ff + d)
    )
    weight = down_weight[0]
    steps = (("y", 4), ("z", 4), ("y", 2), ("z", 2), ("y", 1), ("z", 1), ("c", 1))
    for axis, bit in steps:
        n = lax.axis_size(axis)
        recv = lax.ppermute(weight, axis, [(i, i ^ bit) for i in range(n)])
        low = (lax.axis_index(axis) // bit) % 2 == 0
        weight = jnp.concatenate([jnp.where(low, weight, recv), jnp.where(low, recv, weight)], axis=0)
    weight = weight.reshape(2, 2, 2, 2, 2, 2, 2, -1, d).transpose(6, 4, 2, 5, 3, 1, 0, 7, 8).reshape(ff, d)
    recv = lax.all_to_all(send, "expert", split_axis=0, concat_axis=0, tiled=True).reshape(width, ff + d)
    h_rows = recv[:, :ff]
    g_rows = recv[:, ff:]
    rows_dev = ff // (ny * nz * nc)
    h_perm = h_rows.reshape(width, ny, nz, nc, rows_dev).transpose(0, 3, 2, 1, 4).reshape(width, ff)
    partial_grad = lax.dot_general(
        h_perm, g_rows, (((0,), (0,)), ((), ())), preferred_element_type=jnp.float32
    )
    summed = partial_grad
    for axis, n in (("c", nc), ("z", nz), ("y", ny)):
        parts = lax.all_to_all(
            summed.reshape(n, summed.shape[0] // n, d), axis, split_axis=0, concat_axis=0, tiled=True
        )
        summed = jnp.sum(parts, axis=0)
    summed, weight = lax.optimization_barrier((summed, weight))
    y_rows = jnp.dot(h_rows, weight, preferred_element_type=jnp.float32).astype(jnp.bfloat16)
    dh_rows = lax.dot_general(
        g_rows, weight, (((1,), (1,)), ((), ())), preferred_element_type=jnp.float32
    ).astype(jnp.bfloat16)
    back = lax.all_to_all(
        jnp.concatenate([y_rows, dh_rows], axis=1).reshape(groups, CAP, d + ff),
        "expert",
        split_axis=0,
        concat_axis=0,
        tiled=True,
    ).reshape(width, d + ff)
    output = lax.dot_general(
        placing, back[:, :d], (((0,), (0,)), ((), ())), preferred_element_type=jnp.float32
    ).astype(jnp.bfloat16)
    hidden_grad = lax.dot_general(
        placing, back[:, d:], (((0,), (0,)), ((), ())), preferred_element_type=jnp.float32
    ).astype(jnp.bfloat16)
    return (output, hidden_grad, summed[None])


def solution(mesh):
    ex, dp = mesh.devices.shape
    view = Mesh(mesh.devices.reshape(ex, dp // 16, 8, 2), ("expert",) + DP)
    tokens = P(("expert",) + DP, None)
    placed = (tokens, tokens, tokens, P("expert", DP), P("expert", DP, None))
    return jax.shard_map(
        on_device,
        mesh=view,
        in_specs=placed,
        out_specs=(tokens, tokens, P("expert", DP, None)),
        check_vma=False,
    )
```

```python
import jax
import jax.numpy as jnp
from jax import lax
from jax.sharding import Mesh
from jax.sharding import PartitionSpec as P

CAP = 32
DP = ("y", "z", "c")


def on_device(hidden, cotangent, expert_ids, counts, down_weight):
    tok_rows, ff = hidden.shape
    d = cotangent.shape[1]
    groups = lax.axis_size("expert")
    ny, nz, nc = lax.axis_size("y"), lax.axis_size("z"), lax.axis_size("c")
    width = groups * CAP
    ids = expert_ids[:, 0]
    live = jnp.arange(tok_rows, dtype=jnp.int32) < counts[0, 0]
    member = (ids[:, None] == jnp.arange(groups, dtype=jnp.int32)[None, :]).astype(jnp.int32)
    rank = jnp.sum((jnp.cumsum(member, 0) - 1) * member, 1)
    target = ids * CAP + rank
    placing = jnp.logical_and(
        target[None, :] == jnp.arange(width, dtype=jnp.int32)[:, None], live[None, :]
    ).astype(jnp.bfloat16)
    both = jnp.concatenate([hidden, cotangent], axis=1)
    send = (
        jnp.dot(placing, both, preferred_element_type=jnp.float32)
        .astype(jnp.bfloat16)
        .reshape(groups, CAP, ff + d)
    )
    weight = down_weight[0]
    steps = (("y", 4), ("z", 4), ("y", 2), ("z", 2), ("y", 1), ("z", 1), ("c", 1))
    for axis, bit in steps:
        n = lax.axis_size(axis)
        recv = lax.ppermute(weight, axis, [(i, i ^ bit) for i in range(n)])
        low = (lax.axis_index(axis) // bit) % 2 == 0
        weight = jnp.concatenate([jnp.where(low, weight, recv), jnp.where(low, recv, weight)], axis=0)
    recv = lax.all_to_all(send, "expert", split_axis=0, concat_axis=0, tiled=True).reshape(width, ff + d)
    h_rows = recv[:, :ff]
    g_rows = recv[:, ff:]
    def order(x, axes):
        return x.reshape((width,) + (2,) * 7 + (-1,)).transpose((0,) + axes + (8,)).reshape(width, ff)

    partial_grad = lax.dot_general(
        order(h_rows, (7, 3, 6, 2, 5, 1, 4)), g_rows, (((0,), (0,)), ((), ())),
        preferred_element_type=jnp.float32,
    )
    summed = partial_grad
    for axis, bit in (("c", 1), ("y", 1), ("z", 1), ("y", 2), ("z", 2), ("y", 4), ("z", 4)):
        n = lax.axis_size(axis)
        half = summed.shape[0] // 2
        upper = (lax.axis_index(axis) // bit) % 2
        keep = lax.dynamic_slice_in_dim(summed, upper * half, half)
        send = lax.dynamic_slice_in_dim(summed, (1 - upper) * half, half)
        summed = keep + lax.ppermute(send, axis, [(i, i ^ bit) for i in range(n)])
    summed, weight = lax.optimization_barrier((summed, weight))
    y_rows = jnp.dot(
        order(h_rows, (7, 6, 3, 5, 2, 4, 1)), weight, preferred_element_type=jnp.float32
    ).astype(jnp.bfloat16)
    dh_rows = lax.dot_general(
        g_rows, weight, (((1,), (1,)), ((), ())), preferred_element_type=jnp.float32
    ).astype(jnp.bfloat16)
    dh_rows = order(dh_rows, (7, 5, 3, 6, 4, 2, 1))
    back = lax.all_to_all(
        jnp.concatenate([y_rows, dh_rows], axis=1).reshape(groups, CAP, d + ff),
        "expert",
        split_axis=0,
        concat_axis=0,
        tiled=True,
    ).reshape(width, d + ff)
    output = lax.dot_general(
        placing, back[:, :d], (((0,), (0,)), ((), ())), preferred_element_type=jnp.float32
    ).astype(jnp.bfloat16)
    hidden_grad = lax.dot_general(
        placing, back[:, d:], (((0,), (0,)), ((), ())), preferred_element_type=jnp.float32
    ).astype(jnp.bfloat16)
    return (output, hidden_grad, summed[None])


def solution(mesh):
    ex, dp = mesh.devices.shape
    view = Mesh(mesh.devices.reshape(ex, dp // 16, 8, 2), ("expert",) + DP)
    tokens = P(("expert",) + DP, None)
    placed = (tokens, tokens, tokens, P("expert", DP), P("expert", DP, None))
    return jax.shard_map(
        on_device,
        mesh=view,
        in_specs=placed,
        out_specs=(tokens, tokens, P("expert", DP, None)),
        check_vma=False,
    )
```

```python
import jax
import jax.numpy as jnp
from jax import lax
from jax.sharding import Mesh
from jax.sharding import PartitionSpec as P

CAP = 32
DP = ("y", "z", "c")


def on_device(hidden, cotangent, expert_ids, counts, down_weight):
    tok_rows, ff = hidden.shape
    d = cotangent.shape[1]
    groups = lax.axis_size("expert")
    ny, nz, nc = lax.axis_size("y"), lax.axis_size("z"), lax.axis_size("c")
    width = groups * CAP
    ids = expert_ids[:, 0]
    live = jnp.arange(tok_rows, dtype=jnp.int32) < counts[0, 0]
    member = (ids[:, None] == jnp.arange(groups, dtype=jnp.int32)[None, :]).astype(jnp.int32)
    rank = jnp.sum((jnp.cumsum(member, 0) - 1) * member, 1)
    target = ids * CAP + rank
    placing = jnp.logical_and(
        target[None, :] == jnp.arange(width, dtype=jnp.int32)[:, None], live[None, :]
    ).astype(jnp.bfloat16)
    both = jnp.concatenate([hidden, cotangent], axis=1)
    send = (
        jnp.dot(placing, both, preferred_element_type=jnp.float32)
        .astype(jnp.bfloat16)
        .reshape(groups, CAP, ff + d)
    )
    weight = down_weight[0]
    for axis, bit in (("z", 4), ("y", 4), ("z", 2), ("y", 2), ("z", 1), ("y", 1), ("c", 1)):
        n = lax.axis_size(axis)
        recv = lax.ppermute(weight, axis, [(i, i ^ bit) for i in range(n)])
        low = (lax.axis_index(axis) // bit) % 2 == 0
        weight = jnp.concatenate([jnp.where(low, weight, recv), jnp.where(low, recv, weight)], axis=0)
    recv = lax.all_to_all(send, "expert", split_axis=0, concat_axis=0, tiled=True).reshape(width, ff + d)
    h_rows = recv[:, :ff]
    g_rows = recv[:, ff:]
    rows_dev = ff // (ny * nz * nc)
    h_perm = h_rows.reshape(width, ny, nz, nc, rows_dev).transpose(0, 3, 2, 1, 4).reshape(width, ff)
    partial_grad = lax.dot_general(
        h_perm, g_rows, (((0,), (0,)), ((), ())), preferred_element_type=jnp.float32
    )
    summed = partial_grad
    for axis, n in (("c", nc), ("z", nz), ("y", ny)):
        parts = lax.all_to_all(
            summed.reshape(n, summed.shape[0] // n, d), axis, split_axis=0, concat_axis=0, tiled=True
        )
        summed = jnp.sum(parts, axis=0)
    summed, weight = lax.optimization_barrier((summed, weight))
    def order(x, axes):
        return x.reshape((width,) + (2,) * 7 + (-1,)).transpose((0,) + axes + (8,)).reshape(width, ff)

    y_rows = jnp.dot(
        order(h_rows, (7, 3, 6, 2, 5, 1, 4)), weight, preferred_element_type=jnp.float32
    ).astype(jnp.bfloat16)
    dh_rows = lax.dot_general(
        g_rows, weight, (((1,), (1,)), ((), ())), preferred_element_type=jnp.float32
    ).astype(jnp.bfloat16)
    dh_rows = order(dh_rows, (6, 4, 2, 7, 5, 3, 1))
    back = lax.all_to_all(
        jnp.concatenate([y_rows, dh_rows], axis=1).reshape(groups, CAP, d + ff),
        "expert",
        split_axis=0,
        concat_axis=0,
        tiled=True,
    ).reshape(width, d + ff)
    output = lax.dot_general(
        placing, back[:, :d], (((0,), (0,)), ((), ())), preferred_element_type=jnp.float32
    ).astype(jnp.bfloat16)
    hidden_grad = lax.dot_general(
        placing, back[:, d:], (((0,), (0,)), ((), ())), preferred_element_type=jnp.float32
    ).astype(jnp.bfloat16)
    return (output, hidden_grad, summed[None])


def solution(mesh):
    ex, dp = mesh.devices.shape
    view = Mesh(mesh.devices.reshape(ex, dp // 16, 8, 2), ("expert",) + DP)
    tokens = P(("expert",) + DP, None)
    placed = (tokens, tokens, tokens, P("expert", DP), P("expert", DP, None))
    return jax.shard_map(
        on_device,
        mesh=view,
        in_specs=placed,
        out_specs=(tokens, tokens, P("expert", DP, None)),
        check_vma=False,
    )
```

```python
import jax
import jax.numpy as jnp
from jax import lax
from jax.sharding import Mesh
from jax.sharding import PartitionSpec as P

CAP = 32
DP = ("y", "z", "c")


def on_device(hidden, cotangent, expert_ids, counts, down_weight):
    tok_rows, ff = hidden.shape
    d = cotangent.shape[1]
    groups = lax.axis_size("expert")
    ny, nz, nc = lax.axis_size("y"), lax.axis_size("z"), lax.axis_size("c")
    width = groups * CAP
    ids = expert_ids[:, 0]
    live = jnp.arange(tok_rows, dtype=jnp.int32) < counts[0, 0]
    member = (ids[:, None] == jnp.arange(groups, dtype=jnp.int32)[None, :]).astype(jnp.int32)
    rank = jnp.sum((jnp.cumsum(member, 0) - 1) * member, 1)
    target = ids * CAP + rank
    placing = jnp.logical_and(
        target[None, :] == jnp.arange(width, dtype=jnp.int32)[:, None], live[None, :]
    ).astype(jnp.bfloat16)
    both = jnp.concatenate([hidden, cotangent], axis=1)
    send = (
        jnp.dot(placing, both, preferred_element_type=jnp.float32)
        .astype(jnp.bfloat16)
        .reshape(groups, CAP, ff + d)
    )
    weight = lax.all_gather(down_weight.reshape(1, -1), DP, axis=0, tiled=True).reshape(ff, d)
    recv = lax.all_to_all(send, "expert", split_axis=0, concat_axis=0, tiled=True).reshape(width, ff + d)
    h_rows = recv[:, :ff]
    g_rows = recv[:, ff:]
    rows_dev = ff // (ny * nz * nc)
    h_perm = h_rows.reshape(width, ny, nz, nc, rows_dev).transpose(0, 3, 2, 1, 4).reshape(width, ff)
    partial_grad = lax.dot_general(
        h_perm, g_rows, (((0,), (0,)), ((), ())), preferred_element_type=jnp.float32
    )
    summed = partial_grad
    for axis, n in (("c", nc), ("z", nz), ("y", ny)):
        parts = lax.all_to_all(
            summed.reshape(n, summed.shape[0] // n, d), axis, split_axis=0, concat_axis=0, tiled=True
        )
        summed = jnp.sum(parts, axis=0)
    summed, weight = lax.optimization_barrier((summed, weight))
    y_rows = jnp.dot(h_rows, weight, preferred_element_type=jnp.float32).astype(jnp.bfloat16)
    dh_rows = lax.dot_general(
        g_rows, weight, (((1,), (1,)), ((), ())), preferred_element_type=jnp.float32
    ).astype(jnp.bfloat16)
    back = lax.all_to_all(
        jnp.concatenate([y_rows, dh_rows], axis=1).reshape(groups, CAP, d + ff),
        "expert",
        split_axis=0,
        concat_axis=0,
        tiled=True,
    ).reshape(width, d + ff)
    output = lax.dot_general(
        placing, back[:, :d], (((0,), (0,)), ((), ())), preferred_element_type=jnp.float32
    ).astype(jnp.bfloat16)
    hidden_grad = lax.dot_general(
        placing, back[:, d:], (((0,), (0,)), ((), ())), preferred_element_type=jnp.float32
    ).astype(jnp.bfloat16)
    return (output, hidden_grad, summed[None])


def solution(mesh):
    ex, dp = mesh.devices.shape
    view = Mesh(mesh.devices.reshape(ex, dp // 16, 8, 2), ("expert",) + DP)
    tokens = P(("expert",) + DP, None)
    placed = (tokens, tokens, tokens, P("expert", DP), P("expert", DP, None))
    return jax.shard_map(
        on_device,
        mesh=view,
        in_specs=placed,
        out_specs=(tokens, tokens, P("expert", DP, None)),
        check_vma=False,
    )
```

```python
import jax
import jax.numpy as jnp
from jax import lax
from jax.sharding import Mesh
from jax.sharding import PartitionSpec as P

CAP = 32
DP = ("y", "z", "c")


def on_device(hidden, cotangent, expert_ids, counts, down_weight):
    tok_rows, ff = hidden.shape
    d = cotangent.shape[1]
    groups = lax.axis_size("expert")
    ny, nz, nc = lax.axis_size("y"), lax.axis_size("z"), lax.axis_size("c")
    width = groups * CAP
    ids = expert_ids[:, 0]
    live = jnp.arange(tok_rows, dtype=jnp.int32) < counts[0, 0]
    slots = jnp.arange(tok_rows, dtype=jnp.int32)
    earlier = jnp.logical_and(ids[:, None] == ids[None, :], slots[None, :] < slots[:, None])
    rank = jnp.sum(earlier.astype(jnp.int32), 1)
    target = ids * CAP + rank
    placing = jnp.logical_and(
        target[None, :] == jnp.arange(width, dtype=jnp.int32)[:, None], live[None, :]
    ).astype(jnp.bfloat16)
    both = jnp.concatenate([hidden, cotangent], axis=1)
    send = (
        jnp.dot(placing, both, preferred_element_type=jnp.float32)
        .astype(jnp.bfloat16)
        .reshape(groups, CAP, ff + d)
    )
    weight = lax.all_gather(down_weight, DP, axis=1, tiled=True)[0]
    recv = lax.all_to_all(send, "expert", split_axis=0, concat_axis=0, tiled=True).reshape(width, ff + d)
    h_rows = recv[:, :ff]
    g_rows = recv[:, ff:]
    rows_dev = ff // (ny * nz * nc)
    h_perm = h_rows.reshape(width, ny, nz, nc, rows_dev).transpose(0, 3, 2, 1, 4).reshape(width, ff)
    partial_grad = lax.dot_general(
        h_perm, g_rows, (((0,), (0,)), ((), ())), preferred_element_type=jnp.float32
    )
    summed = partial_grad
    for axis, n in (("c", nc), ("z", nz), ("y", ny)):
        parts = lax.all_to_all(
            summed.reshape(n, summed.shape[0] // n, d), axis, split_axis=0, concat_axis=0, tiled=True
        )
        summed = jnp.sum(parts, axis=0)
    summed, weight = lax.optimization_barrier((summed, weight))
    y_rows = jnp.dot(h_rows, weight, preferred_element_type=jnp.float32).astype(jnp.bfloat16)
    dh_rows = lax.dot_general(
        g_rows, weight, (((1,), (1,)), ((), ())), preferred_element_type=jnp.float32
    ).astype(jnp.bfloat16)
    back = lax.all_to_all(
        jnp.concatenate([y_rows, dh_rows], axis=1).reshape(groups, CAP, d + ff),
        "expert",
        split_axis=0,
        concat_axis=0,
        tiled=True,
    ).reshape(width, d + ff)
    output = lax.dot_general(
        placing, back[:, :d], (((0,), (0,)), ((), ())), preferred_element_type=jnp.float32
    ).astype(jnp.bfloat16)
    hidden_grad = lax.dot_general(
        placing, back[:, d:], (((0,), (0,)), ((), ())), preferred_element_type=jnp.float32
    ).astype(jnp.bfloat16)
    return (output, hidden_grad, summed[None])


def solution(mesh):
    ex, dp = mesh.devices.shape
    view = Mesh(mesh.devices.reshape(ex, dp // 16, 8, 2), ("expert",) + DP)
    tokens = P(("expert",) + DP, None)
    placed = (tokens, tokens, tokens, P("expert", DP), P("expert", DP, None))
    return jax.shard_map(
        on_device,
        mesh=view,
        in_specs=placed,
        out_specs=(tokens, tokens, P("expert", DP, None)),
        check_vma=False,
    )
```

```python
import jax
import jax.numpy as jnp
from jax import lax
from jax.sharding import Mesh
from jax.sharding import PartitionSpec as P

CAP = 32
DP = ("y", "z", "c")


def on_device(hidden, cotangent, expert_ids, counts, down_weight):
    tok_rows, ff = hidden.shape
    d = cotangent.shape[1]
    groups = lax.axis_size("expert")
    ny, nz, nc = lax.axis_size("y"), lax.axis_size("z"), lax.axis_size("c")
    width = groups * CAP
    ids = expert_ids[:, 0]
    live = jnp.arange(tok_rows, dtype=jnp.int32) < counts[0, 0]
    slots = jnp.arange(tok_rows, dtype=jnp.int32)
    earlier = jnp.logical_and(ids[:, None] == ids[None, :], slots[None, :] < slots[:, None])
    rank = jnp.sum(earlier.astype(jnp.int32), 1)
    target = ids * CAP + rank
    placing = jnp.logical_and(
        target[None, :] == jnp.arange(width, dtype=jnp.int32)[:, None], live[None, :]
    ).astype(jnp.bfloat16)
    both = jnp.concatenate([hidden, cotangent], axis=1)
    send = (
        jnp.dot(placing, both, preferred_element_type=jnp.float32)
        .astype(jnp.bfloat16)
        .reshape(groups, CAP, ff + d)
    )
    weight = lax.all_gather(down_weight, DP, axis=1, tiled=True)[0]
    recv = lax.all_to_all(send, "expert", split_axis=0, concat_axis=0, tiled=True).reshape(width, ff + d)
    h_rows = recv[:, :ff]
    g_rows = recv[:, ff:]
    rows_dev = ff // (ny * nz * nc)
    h_perm = h_rows.reshape(width, ny, nz, nc, rows_dev).transpose(0, 3, 2, 1, 4).reshape(width, ff)
    partial_grad = lax.dot_general(
        h_perm, g_rows, (((0,), (0,)), ((), ())), preferred_element_type=jnp.float32
    )
    summed = partial_grad
    for axis, n in (("c", nc), ("z", nz), ("y", ny)):
        parts = lax.all_to_all(
            summed.reshape(n, summed.shape[0] // n, d), axis, split_axis=0, concat_axis=0, tiled=True
        )
        summed = jnp.sum(parts, axis=0)
    summed, weight = lax.optimization_barrier((summed, weight))
    y_rows = jnp.dot(h_rows, weight, preferred_element_type=jnp.float32).astype(jnp.bfloat16)
    dh_rows = lax.dot_general(
        g_rows, weight, (((1,), (1,)), ((), ())), preferred_element_type=jnp.float32
    ).astype(jnp.bfloat16)
    back = lax.all_to_all(
        jnp.concatenate([y_rows, dh_rows], axis=1).reshape(groups, CAP, d + ff),
        "expert",
        split_axis=0,
        concat_axis=0,
        tiled=True,
    ).reshape(width, d + ff)
    placed_back = lax.dot_general(
        placing, back, (((0,), (0,)), ((), ())), preferred_element_type=jnp.float32
    ).astype(jnp.bfloat16)
    output = placed_back[:, :d]
    hidden_grad = placed_back[:, d:]
    return (output, hidden_grad, summed[None])


def solution(mesh):
    ex, dp = mesh.devices.shape
    view = Mesh(mesh.devices.reshape(ex, dp // 16, 8, 2), ("expert",) + DP)
    tokens = P(("expert",) + DP, None)
    placed = (tokens, tokens, tokens, P("expert", DP), P("expert", DP, None))
    return jax.shard_map(
        on_device,
        mesh=view,
        in_specs=placed,
        out_specs=(tokens, tokens, P("expert", DP, None)),
        check_vma=False,
    )
```

```python
import jax
import jax.numpy as jnp
from jax import lax
from jax.sharding import Mesh
from jax.sharding import PartitionSpec as P

CAP = 32
DP = ("y", "z", "c")


def on_device(hidden, cotangent, expert_ids, counts, down_weight):
    tok_rows, ff = hidden.shape
    d = cotangent.shape[1]
    groups = lax.axis_size("expert")
    ny, nz, nc = lax.axis_size("y"), lax.axis_size("z"), lax.axis_size("c")
    width = groups * CAP
    ids = expert_ids[:, 0]
    live = jnp.arange(tok_rows, dtype=jnp.int32) < counts[0, 0]
    slots = jnp.arange(tok_rows, dtype=jnp.int32)
    earlier = jnp.logical_and(ids[:, None] == ids[None, :], slots[None, :] < slots[:, None])
    rank = jnp.sum(earlier.astype(jnp.int32), 1)
    target = ids * CAP + rank
    placing = jnp.logical_and(
        target[None, :] == jnp.arange(width, dtype=jnp.int32)[:, None], live[None, :]
    ).astype(jnp.bfloat16)
    both = jnp.concatenate([hidden, cotangent], axis=1)
    send = (
        jnp.dot(placing, both, preferred_element_type=jnp.float32)
        .astype(jnp.bfloat16)
        .reshape(groups, CAP, ff + d)
    )
    weight_t = lax.all_gather(down_weight[0].T, DP, axis=1, tiled=True)
    recv = lax.all_to_all(send, "expert", split_axis=0, concat_axis=0, tiled=True).reshape(width, ff + d)
    h_rows = recv[:, :ff]
    g_rows = recv[:, ff:]
    rows_dev = ff // (ny * nz * nc)
    h_perm = h_rows.reshape(width, ny, nz, nc, rows_dev).transpose(0, 3, 2, 1, 4).reshape(width, ff)
    partial_grad = lax.dot_general(
        h_perm, g_rows, (((0,), (0,)), ((), ())), preferred_element_type=jnp.float32
    )
    summed = partial_grad
    for axis, n in (("c", nc), ("z", nz), ("y", ny)):
        parts = lax.all_to_all(
            summed.reshape(n, summed.shape[0] // n, d), axis, split_axis=0, concat_axis=0, tiled=True
        )
        summed = jnp.sum(parts, axis=0)
    summed, weight_t = lax.optimization_barrier((summed, weight_t))
    y_rows = lax.dot_general(
        h_rows, weight_t, (((1,), (1,)), ((), ())), preferred_element_type=jnp.float32
    ).astype(jnp.bfloat16)
    dh_rows = jnp.dot(g_rows, weight_t, preferred_element_type=jnp.float32).astype(jnp.bfloat16)
    back = lax.all_to_all(
        jnp.concatenate([y_rows, dh_rows], axis=1).reshape(groups, CAP, d + ff),
        "expert",
        split_axis=0,
        concat_axis=0,
        tiled=True,
    ).reshape(width, d + ff)
    placed_back = lax.dot_general(
        placing, back, (((0,), (0,)), ((), ())), preferred_element_type=jnp.float32
    ).astype(jnp.bfloat16)
    output = placed_back[:, :d]
    hidden_grad = placed_back[:, d:]
    return (output, hidden_grad, summed[None])


def solution(mesh):
    ex, dp = mesh.devices.shape
    view = Mesh(mesh.devices.reshape(ex, dp // 16, 8, 2), ("expert",) + DP)
    tokens = P(("expert",) + DP, None)
    placed = (tokens, tokens, tokens, P("expert", DP), P("expert", DP, None))
    return jax.shard_map(
        on_device,
        mesh=view,
        in_specs=placed,
        out_specs=(tokens, tokens, P("expert", DP, None)),
        check_vma=False,
    )
```
